32 devices in a mesh: store: 4 (over x, core), blk: 2 (over y), batch: 4 (over z).
Axes of the slice: x: 2, y: 2, z: 4, core: 2. Of those that a mesh axis runs over, the one named last changes fastest.
Arguments:
- cands: bfloat16 [16, 256, 1024], P(('batch', 'store'), 'blk'), parts along dimension 0, may hold values from -6 to 6
- kv_store: bfloat16 [16, 512, 2, 1024], P('batch', ('blk', 'store')), parts along dimension 0, may hold values from -6 to 6
- proj_weight: bfloat16 [1024, 2, 1024], P(None, None, 'blk'), may hold values from -0.1875 to 0.1875
- norm_gain: float32 [1024], replicated, may hold values from 0.5 to 1.5
- users: int32 [16], P('batch'), parts along dimension 0, may hold values from 0 to 3, each once
- lengths: int32 [16], P('batch'), parts along dimension 0, may hold values from 128 to 512, as said below
Outputs:
- scored: bfloat16 [16, 256, 1024], P(('batch', 'store'), 'blk'), parts along dimension 0
The draws below stay inside these ranges and needn't reach their ends.
There are 4 independent parts, one for each index of `batch`. The reference program is written for one: setup_inputs(seed, part) draws one part's arguments, and reference() takes and returns one part's arrays. A program takes and returns all parts, laid end to end along the dimension named above; an argument that names none is the same for every part. Nothing has to cross between parts.
Inputs may be any that keep to these rules, and one draw needn't show every extreme that they name: A permutation of the users. `lengths`: some user has all 512 events live.
All inputs are finite; a program needn't handle non-finite values.
Results may differ from the reference program's by a relative error of at most 0.014.
Values may be sent and summed in bfloat16 or wider, within the bound.
No kernel may reach another device: no remote copies, remote signals or barrier semaphores. Data moves between devices by JAX's collectives and lax.ppermute only.
A program may use at most 64 MiB of HBM per device.

```python
import jax
import jax.numpy as jnp
from jax import lax

D = 1024
HEADS = 8
CAND = 256
HIST = 512
USERS = 4


def draw_lengths(key, part):
    first, second = jax.random.split(jax.random.fold_in(key, 7))
    values = jax.random.randint(first, (USERS,), HIST // 4, HIST + 1)
    chosen = jax.random.randint(second, (), 0, USERS)
    return jnp.where(jnp.arange(USERS) == chosen, HIST, values).astype(jnp.int32)


def shard_levels(rng, extent, cuts, least, high):
    level, own = 1.0, jax.random.fold_in(rng, 6)
    for axis_at, parts in cuts:
        draws = jnp.exp(jax.random.uniform(jax.random.fold_in(own, axis_at), (parts,), jnp.float32, least / len(cuts), high / len(cuts)))
        level = level * jnp.repeat(draws, extent[axis_at] // parts).reshape([-1 if axis == axis_at else 1 for axis in range(len(extent))])
    return level


def normal_values(key, extent, scale, limit, cuts=(), kind=jnp.bfloat16):
    drawn = jax.random.normal(key, extent, jnp.float32) * scale
    if len(cuts) > 0:
        drawn = shard_levels(key, extent, cuts, -0.22, 0.18) * drawn
    return jnp.clip(drawn, min=-limit, max=limit).astype(kind)


def setup_inputs(seed: int = 0, part: int = 0) -> dict:
    key_of = jax.random.split(jax.random.key(seed), 7)
    part_keys = jax.random.split(jax.random.fold_in(key_of[6], part), 7)
    cands = normal_values(part_keys[0], (USERS, CAND, D), 1.0, 6.0, ((0, 4), (1, 2)))
    kv_store = normal_values(part_keys[1], (USERS, HIST, 2, D), 1.0, 6.0, ((1, 8),))
    proj_weight = normal_values(key_of[2], (D, 2, D), D ** -0.5, 0.1875, ((2, 2),))
    norm_gain = jnp.clip(1.0 + 0.1 * jax.random.normal(key_of[3], (D,), jnp.float32), 0.5, 1.5)
    users = jax.random.permutation(part_keys[4], USERS).astype(jnp.int32)
    lengths = draw_lengths(jax.random.fold_in(jax.random.fold_in(key_of[6], part), 71), part)
    return {"cands": cands, "kv_store": kv_store, "proj_weight": proj_weight, "norm_gain": norm_gain, "users": users, "lengths": lengths}


def reference(cands, kv_store, proj_weight, norm_gain, users, lengths):
    head_size = D // HEADS
    inverse = head_size ** (-0.5)
    weight_flat = proj_weight.reshape(D, 2 * D)

    def one_user(slot):
        person = lax.dynamic_index_in_dim(users, slot, 0, keepdims=False)
        count = lax.dynamic_index_in_dim(lengths, person, 0, keepdims=False)
        feats = lax.dynamic_index_in_dim(cands, slot, 0, keepdims=False)
        hist = lax.dynamic_index_in_dim(kv_store, person, 0, keepdims=False)
        proj = jnp.dot(feats, weight_flat, preferred_element_type=jnp.float32)
        query = proj[:, :D].astype(jnp.bfloat16)
        gate = jax.nn.silu(proj[:, D:]).astype(jnp.bfloat16)
        keys = hist[:, 0, :].reshape(HIST, HEADS, head_size).astype(jnp.float32)
        values = hist[:, 1, :].reshape(HIST, HEADS, head_size).astype(jnp.float32)
        qheads = query.reshape(CAND, HEADS, head_size).astype(jnp.float32)
        scores = jnp.einsum('chd,khd->hck', qheads, keys) * inverse
        live = (jnp.arange(HIST) < count).astype(jnp.float32)
        weights = (jax.nn.silu(scores) * live[None, None, :] / count.astype(jnp.float32)).astype(jnp.bfloat16)
        attended = jnp.einsum('hck,khd->chd', weights.astype(jnp.float32), values).reshape(CAND, D)
        attended = attended.astype(jnp.bfloat16).astype(jnp.float32)
        mean = lax.optimization_barrier(jnp.mean(attended, axis=1, keepdims=True))
        var = lax.optimization_barrier(jnp.mean((attended - mean) ** 2, axis=1, keepdims=True))
        normed = (attended - mean) * lax.rsqrt(var + 1e-05) * norm_gain[None, :]
        return (normed * gate.astype(jnp.float32)).astype(jnp.bfloat16)
    return lax.map(one_user, jnp.arange(USERS, dtype=jnp.int32))
```

```python
import jax
import jax.numpy as jnp
from jax import lax
from jax.sharding import PartitionSpec as P

D = 1024
HEADS = 8


def attend(query, keys, values, count):
    head_size = D // HEADS
    inverse = head_size ** (-0.5)
    rows = query.shape[0]
    local_heads = query.shape[1] // head_size
    total = keys.shape[0]
    block = min(total, 512)
    qheads = query.reshape(rows, local_heads, head_size)
    scale_count = count.astype(jnp.float32)

    def one_block(index, accum):
        start = index * block
        key_block = lax.dynamic_slice_in_dim(keys, start, block, 0).reshape(
            block, local_heads, head_size
        )
        value_block = lax.dynamic_slice_in_dim(values, start, block, 0).reshape(
            block, local_heads, head_size
        )
        scores = (
            jnp.einsum("chd,khd->hck", qheads, key_block, preferred_element_type=jnp.float32)
            * inverse
        )
        live = (start + jnp.arange(block) < count).astype(jnp.float32)
        weights = (jax.nn.silu(scores) * live[None, None, :] / scale_count).astype(jnp.bfloat16)
        part_sum = jnp.einsum(
            "hck,khd->chd", weights, value_block, preferred_element_type=jnp.float32
        )
        return accum + part_sum.reshape(rows, local_heads * head_size)

    empty = jnp.zeros((rows, local_heads * head_size), jnp.float32)
    steps = total // block
    if steps == 1:
        return one_block(0, empty)
    return lax.fori_loop(0, steps, one_block, empty)


def finish(attended, gate, norm_gain):
    wide = attended.astype(jnp.float32)
    mean = jnp.mean(wide, axis=1, keepdims=True)
    var = jnp.mean((wide - mean) ** 2, axis=1, keepdims=True)
    normed = (wide - mean) * lax.rsqrt(var + 1e-05) * norm_gain[None, :]
    return (normed * gate.astype(jnp.float32)).astype(jnp.bfloat16)


def per_device(cands, kv_store, proj_weight, norm_gain, users, lengths):
    n_blk = lax.axis_size("blk")
    slot = lax.axis_index("store")
    person = lax.dynamic_index_in_dim(users, slot, 0, keepdims=False)
    count = lax.dynamic_index_in_dim(lengths, person, 0, keepdims=False)
    width = proj_weight.shape[0]
    half = proj_weight.shape[2]

    ordered = jnp.take(kv_store, users, axis=0)
    n_users, n_pos = ordered.shape[0], ordered.shape[1]
    ordered = ordered.reshape(n_users, n_pos, 2, n_blk, half)
    ordered = jnp.transpose(ordered, (3, 0, 1, 2, 4)).reshape(n_blk * n_users, n_pos, 2, half)
    fetched = lax.all_to_all(
        ordered, ("blk", "store"), split_axis=0, concat_axis=1, tiled=True
    )
    keys = fetched[0, :, 0, :]
    values = fetched[0, :, 1, :]

    feats = lax.all_gather(cands[0], "blk", axis=0, tiled=True)
    proj = jnp.dot(
        feats, proj_weight.reshape(width, 2 * half), preferred_element_type=jnp.float32
    )
    query = proj[:, :half].astype(jnp.bfloat16)
    gate = jax.nn.silu(proj[:, half:]).astype(jnp.bfloat16)

    attended = attend(query, keys, values, count).astype(jnp.bfloat16)
    rows = attended.shape[0] // n_blk
    both = jnp.stack([attended, gate]).reshape(2, n_blk, rows, half)
    mine = lax.all_to_all(both, "blk", split_axis=1, concat_axis=3, tiled=True)
    mine = mine.reshape(2, rows, n_blk * half)
    return finish(mine[0], mine[1], norm_gain)[None]


def solution(mesh):
    in_specs = (
        P(("batch", "store"), "blk", None),
        P("batch", ("blk", "store"), None, None),
        P(None, None, "blk"),
        P(),
        P("batch"),
        P("batch"),
    )
    out_specs = P(("batch", "store"), "blk", None)
    return jax.shard_map(
        per_device, mesh=mesh, in_specs=in_specs, out_specs=out_specs, check_vma=False
    )
```

```python
import jax
import jax.numpy as jnp
from jax import lax
from jax.sharding import PartitionSpec as P
from jax.experimental import pallas as pl
from jax.experimental.pallas import tpu as pltpu

D = 1024
HEADS = 8


def attend(query, keys, values, count):
    head_size = D // HEADS
    inverse = head_size ** (-0.5)
    rows = query.shape[0]
    local_heads = query.shape[1] // head_size
    total = keys.shape[0]
    block = min(total, 512)
    qheads = query.reshape(rows, local_heads, head_size)
    scale_count = count.astype(jnp.float32)

    def one_block(index, accum):
        start = index * block
        key_block = lax.dynamic_slice_in_dim(keys, start, block, 0).reshape(
            block, local_heads, head_size
        )
        value_block = lax.dynamic_slice_in_dim(values, start, block, 0).reshape(
            block, local_heads, head_size
        )
        scores = (
            jnp.einsum("chd,khd->hck", qheads, key_block, preferred_element_type=jnp.float32)
            * inverse
        )
        live = (start + jnp.arange(block) < count).astype(jnp.float32)
        weights = (jax.nn.silu(scores) * live[None, None, :] / scale_count).astype(jnp.bfloat16)
        part_sum = jnp.einsum(
            "hck,khd->chd", weights, value_block, preferred_element_type=jnp.float32
        )
        return accum + part_sum.reshape(rows, local_heads * head_size)

    empty = jnp.zeros((rows, local_heads * head_size), jnp.float32)
    steps = total // block
    if steps == 1:
        return one_block(0, empty)
    return lax.fori_loop(0, steps, one_block, empty)


def finish(attended, gate, norm_gain):
    wide = attended.astype(jnp.float32)
    mean = jnp.mean(wide, axis=1, keepdims=True)
    var = jnp.mean((wide - mean) ** 2, axis=1, keepdims=True)
    normed = (wide - mean) * lax.rsqrt(var + 1e-05) * norm_gain[None, :]
    return (normed * gate.astype(jnp.float32)).astype(jnp.bfloat16)


def gather_kv(kv_store, users, n_blk):
    n_users, n_pos, two, width = kv_store.shape
    half = width // n_blk
    targets = n_blk * n_users

    def kernel(users_ref, kv_hbm, out_hbm, sems):
        def start(t, carry):
            b = t // n_users
            s = t % n_users
            pltpu.make_async_copy(
                kv_hbm.at[users_ref[s], :, :, pl.ds(pl.multiple_of(b * half, 128), half)],
                out_hbm.at[t],
                sems.at[t],
            ).start()
            return carry

        def wait(t, carry):
            pltpu.make_async_copy(
                kv_hbm.at[0, :, :, pl.ds(0, half)], out_hbm.at[t], sems.at[t]
            ).wait()
            return carry

        lax.fori_loop(0, targets, start, 0)
        lax.fori_loop(0, targets, wait, 0)

    return pl.pallas_call(
        kernel,
        out_shape=jax.ShapeDtypeStruct((targets, n_pos, two, half), kv_store.dtype),
        grid_spec=pltpu.PrefetchScalarGridSpec(
            num_scalar_prefetch=1,
            grid=(1,),
            in_specs=[pl.BlockSpec(memory_space=pl.ANY)],
            out_specs=pl.BlockSpec(memory_space=pl.ANY),
            scratch_shapes=[pltpu.SemaphoreType.DMA((targets,))],
        ),
    )(users, kv_store)


def per_device(cands, kv_store, proj_weight, norm_gain, users, lengths):
    n_blk = lax.axis_size("blk")
    blk = lax.axis_index("blk")
    slot = lax.axis_index("store")
    person = lax.dynamic_index_in_dim(users, slot, 0, keepdims=False)
    count = lax.dynamic_index_in_dim(lengths, person, 0, keepdims=False)
    half = proj_weight.shape[2]

    ordered = gather_kv(kv_store, users, n_blk)
    fetched = lax.all_to_all(
        ordered, ("blk", "store"), split_axis=0, concat_axis=1, tiled=True
    )
    keys = fetched[0, :, 0, :]
    values = fetched[0, :, 1, :]

    mine = cands[0]
    rows = mine.shape[0]
    if n_blk == 2:
        swap = [(0, 1), (1, 0)]
        peer = lax.ppermute(mine, "blk", swap)
        proj = jnp.einsum(
            "cd,dkh->kch", jnp.concatenate([peer, mine]), proj_weight,
            preferred_element_type=jnp.float32,
        )
        query = proj[0].astype(jnp.bfloat16)
        gate = jax.nn.silu(proj[1]).astype(jnp.bfloat16)
        sent = attend(query[:rows], keys, values, count).astype(jnp.bfloat16)
        back = lax.ppermute(jnp.stack([sent, gate[:rows]]), "blk", swap)
        kept = attend(query[rows:], keys, values, count).astype(jnp.bfloat16)
        first = blk == 0
        attended = jnp.where(first, jnp.concatenate([kept, back[0]], axis=1),
                             jnp.concatenate([back[0], kept], axis=1))
        gate_own = jnp.where(first, jnp.concatenate([gate[rows:], back[1]], axis=1),
                             jnp.concatenate([back[1], gate[rows:]], axis=1))
        return finish(attended, gate_own, norm_gain)[None]

    feats = lax.all_gather(mine, "blk", axis=0, tiled=True)
    proj = jnp.einsum("cd,dkh->kch", feats, proj_weight, preferred_element_type=jnp.float32)
    query = proj[0].astype(jnp.bfloat16)
    gate = jax.nn.silu(proj[1]).astype(jnp.bfloat16)
    attended = attend(query, keys, values, count).astype(jnp.bfloat16)
    both = jnp.stack([attended, gate]).reshape(2, n_blk, rows, half)
    own = lax.all_to_all(both, "blk", split_axis=1, concat_axis=3, tiled=True)
    own = own.reshape(2, rows, n_blk * half)
    return finish(own[0], own[1], norm_gain)[None]


def solution(mesh):
    in_specs = (
        P(("batch", "store"), "blk", None),
        P("batch", ("blk", "store"), None, None),
        P(None, None, "blk"),
        P(),
        P("batch"),
        P("batch"),
    )
    out_specs = P(("batch", "store"), "blk", None)
    return jax.shard_map(
        per_device, mesh=mesh, in_specs=in_specs, out_specs=out_specs, check_vma=False
    )
```

```python
import jax
import jax.numpy as jnp
from jax import lax
from jax.sharding import PartitionSpec as P

D = 1024
HEADS = 8
HEAD_SIZE = D // HEADS


def attend(qheads, keys, values, count):
    inverse = HEAD_SIZE ** (-0.5)
    local_heads, rows, _ = qheads.shape
    total = keys.shape[1]
    block = min(total, 512)
    scale_count = count.astype(jnp.float32)

    def one_block(index, accum):
        start = index * block
        key_block = lax.dynamic_slice_in_dim(keys, start, block, 1)
        value_block = lax.dynamic_slice_in_dim(values, start, block, 1)
        scores = (
            jnp.einsum("hcd,hkd->hck", qheads, key_block, preferred_element_type=jnp.float32)
            * inverse
        )
        live = (start + jnp.arange(block) < count).astype(jnp.float32)
        weights = (jax.nn.silu(scores) * live[None, None, :] / scale_count).astype(jnp.bfloat16)
        part_sum = jnp.einsum(
            "hck,hkd->chd", weights, value_block, preferred_element_type=jnp.float32
        )
        return accum + part_sum.reshape(rows, local_heads * HEAD_SIZE)

    empty = jnp.zeros((rows, local_heads * HEAD_SIZE), jnp.float32)
    steps = total // block
    if steps == 1:
        return one_block(0, empty)
    return lax.fori_loop(0, steps, one_block, empty)


def finish(attended, gate, norm_gain):
    wide = attended.astype(jnp.float32)
    mean = jnp.mean(wide, axis=1, keepdims=True)
    var = jnp.mean((wide - mean) ** 2, axis=1, keepdims=True)
    normed = (wide - mean) * lax.rsqrt(var + 1e-05) * norm_gain[None, :]
    return (normed * gate.astype(jnp.float32)).astype(jnp.bfloat16)


def per_device(cands, kv_store, proj_weight, norm_gain, users, lengths):
    n_blk = lax.axis_size("blk")
    blk = lax.axis_index("blk")
    slot = lax.axis_index("store")
    person = lax.dynamic_index_in_dim(users, slot, 0, keepdims=False)
    count = lax.dynamic_index_in_dim(lengths, person, 0, keepdims=False)
    half = proj_weight.shape[2]
    local_heads = half // HEAD_SIZE

    n_users, n_pos = kv_store.shape[0], kv_store.shape[1]
    ordered = jnp.take(kv_store, users, axis=0).reshape(
        n_users, n_pos, 2, n_blk, local_heads, HEAD_SIZE
    )
    ordered = jnp.transpose(ordered, (3, 0, 2, 4, 1, 5)).reshape(
        n_blk * n_users, 2, local_heads, n_pos, HEAD_SIZE
    )
    fetched = lax.all_to_all(
        ordered, ("blk", "store"), split_axis=0, concat_axis=3, tiled=True
    )
    keys = fetched[0, 0]
    values = fetched[0, 1]

    mine = cands[0]
    rows = mine.shape[0]

    def project(feats):
        proj = jnp.einsum("cd,dkh->kch", feats, proj_weight, preferred_element_type=jnp.float32)
        query = proj[0].astype(jnp.bfloat16).reshape(-1, local_heads, HEAD_SIZE)
        gate = jax.nn.silu(proj[1]).astype(jnp.bfloat16)
        return jnp.transpose(query, (1, 0, 2)), gate

    if n_blk == 2:
        swap = [(0, 1), (1, 0)]
        peer = lax.ppermute(mine, "blk", swap)
        query_own, gate_own = project(mine)
        query_peer, gate_peer = project(peer)
        sent = attend(query_peer, keys, values, count).astype(jnp.bfloat16)
        back = lax.ppermute(jnp.stack([sent, gate_peer]), "blk", swap)
        kept = attend(query_own, keys, values, count).astype(jnp.bfloat16)
        first = blk == 0
        attended = jnp.where(first, jnp.concatenate([kept, back[0]], axis=1),
                             jnp.concatenate([back[0], kept], axis=1))
        gate_full = jnp.where(first, jnp.concatenate([gate_own, back[1]], axis=1),
                              jnp.concatenate([back[1], gate_own], axis=1))
        return finish(attended, gate_full, norm_gain)[None]

    feats = lax.all_gather(mine, "blk", axis=0, tiled=True)
    query, gate = project(feats)
    attended = attend(query, keys, values, count).astype(jnp.bfloat16)
    both = jnp.stack([attended, gate]).reshape(2, n_blk, rows, half)
    own = lax.all_to_all(both, "blk", split_axis=1, concat_axis=3, tiled=True)
    own = own.reshape(2, rows, n_blk * half)
    return finish(own[0], own[1], norm_gain)[None]


def solution(mesh):
    in_specs = (
        P(("batch", "store"), "blk", None),
        P("batch", ("blk", "store"), None, None),
        P(None, None, "blk"),
        P(),
        P("batch"),
        P("batch"),
    )
    out_specs = P(("batch", "store"), "blk", None)
    return jax.shard_map(
        per_device, mesh=mesh, in_specs=in_specs, out_specs=out_specs, check_vma=False
    )
```

```python
import jax
import jax.numpy as jnp
from jax import lax
from jax.sharding import PartitionSpec as P

D = 1024
HEADS = 8
HEAD_SIZE = D // HEADS


def attend(qheads, keys, values, count):
    inverse = HEAD_SIZE ** (-0.5)
    local_heads, rows, _ = qheads.shape
    total = keys.shape[1]
    block = min(total, 512)
    scale_count = count.astype(jnp.float32)

    def one_block(index, accum):
        start = index * block
        key_block = lax.dynamic_slice_in_dim(keys, start, block, 1)
        value_block = lax.dynamic_slice_in_dim(values, start, block, 1)
        scores = (
            jnp.einsum("hcd,hkd->hck", qheads, key_block, preferred_element_type=jnp.float32)
            * inverse
        )
        live = (start + jnp.arange(block) < count).astype(jnp.float32)
        weights = (jax.nn.silu(scores) * live[None, None, :] / scale_count).astype(jnp.bfloat16)
        part_sum = jnp.einsum(
            "hck,hkd->chd", weights, value_block, preferred_element_type=jnp.float32
        )
        return accum + part_sum.reshape(rows, local_heads * HEAD_SIZE)

    empty = jnp.zeros((rows, local_heads * HEAD_SIZE), jnp.float32)
    steps = total // block
    if steps == 1:
        return one_block(0, empty)
    return lax.fori_loop(0, steps, one_block, empty)


def finish(attended, gate, norm_gain):
    wide = attended.astype(jnp.float32)
    mean = jnp.mean(wide, axis=1, keepdims=True)
    var = jnp.mean((wide - mean) ** 2, axis=1, keepdims=True)
    normed = (wide - mean) * lax.rsqrt(var + 1e-05) * norm_gain[None, :]
    return (normed * gate.astype(jnp.float32)).astype(jnp.bfloat16)


def per_device(cands, kv_store, proj_weight, norm_gain, users, lengths):
    n_blk = lax.axis_size("blk")
    blk = lax.axis_index("blk")
    slot = lax.axis_index("store")
    person = lax.dynamic_index_in_dim(users, slot, 0, keepdims=False)
    count = lax.dynamic_index_in_dim(lengths, person, 0, keepdims=False)
    half = proj_weight.shape[2]
    local_heads = half // HEAD_SIZE

    n_users, n_pos = kv_store.shape[0], kv_store.shape[1]
    ordered = kv_store.at[users].get(mode="promise_in_bounds", unique_indices=True).reshape(
        n_users, n_pos, 2, n_blk, local_heads, HEAD_SIZE
    )
    ordered = jnp.transpose(ordered, (3, 0, 2, 4, 1, 5)).reshape(
        n_blk * n_users, 2, local_heads, n_pos, HEAD_SIZE
    )
    fetched = lax.all_to_all(
        ordered, ("blk", "store"), split_axis=0, concat_axis=3, tiled=True
    )
    keys = fetched[0, 0]
    values = fetched[0, 1]

    mine = cands[0]
    rows = mine.shape[0]

    def project(feats):
        proj = jnp.einsum("cd,dkh->ckh", feats, proj_weight, preferred_element_type=jnp.float32).transpose(1, 0, 2)
        query = proj[0].astype(jnp.bfloat16).reshape(-1, local_heads, HEAD_SIZE)
        gate = jax.nn.silu(proj[1]).astype(jnp.bfloat16)
        return jnp.transpose(query, (1, 0, 2)), gate

    if n_blk == 2:
        swap = [(0, 1), (1, 0)]
        peer = lax.ppermute(mine, "blk", swap)
        query_own, gate_own = project(mine)
        query_peer, gate_peer = project(peer)
        sent = attend(query_peer, keys, values, count).astype(jnp.bfloat16)
        back = lax.ppermute(jnp.stack([sent, gate_peer]), "blk", swap)
        kept = attend(query_own, keys, values, count).astype(jnp.bfloat16)
        first = blk == 0
        attended = jnp.where(first, jnp.concatenate([kept, back[0]], axis=1),
                             jnp.concatenate([back[0], kept], axis=1))
        gate_full = jnp.where(first, jnp.concatenate([gate_own, back[1]], axis=1),
                              jnp.concatenate([back[1], gate_own], axis=1))
        return finish(attended, gate_full, norm_gain)[None]

    feats = lax.all_gather(mine, "blk", axis=0, tiled=True)
    query, gate = project(feats)
    attended = attend(query, keys, values, count).astype(jnp.bfloat16)
    both = jnp.stack([attended, gate]).reshape(2, n_blk, rows, half)
    own = lax.all_to_all(both, "blk", split_axis=1, concat_axis=3, tiled=True)
    own = own.reshape(2, rows, n_blk * half)
    return finish(own[0], own[1], norm_gain)[None]


def solution(mesh):
    in_specs = (
        P(("batch", "store"), "blk", None),
        P("batch", ("blk", "store"), None, None),
        P(None, None, "blk"),
        P(),
        P("batch"),
        P("batch"),
    )
    out_specs = P(("batch", "store"), "blk", None)
    return jax.shard_map(
        per_device, mesh=mesh, in_specs=in_specs, out_specs=out_specs, check_vma=False
    )
```

```python
import jax
import jax.numpy as jnp
from jax import lax
from jax.sharding import PartitionSpec as P

D = 1024
HEADS = 8
HEAD_SIZE = D // HEADS


def attend(qheads, keys, values, count):
    inverse = HEAD_SIZE ** (-0.5)
    local_heads, rows, _ = qheads.shape
    total = keys.shape[1]
    block = min(total, 512)
    scale_count = count.astype(jnp.float32)

    def one_block(index, accum):
        start = index * block
        key_block = lax.dynamic_slice_in_dim(keys, start, block, 1)
        value_block = lax.dynamic_slice_in_dim(values, start, block, 1)
        scores = (
            jnp.einsum("hcd,hkd->hck", qheads, key_block, preferred_element_type=jnp.float32)
            * inverse
        )
        live = (start + jnp.arange(block) < count).astype(jnp.float32)
        weights = (jax.nn.silu(scores) * live[None, None, :] / scale_count).astype(jnp.bfloat16)
        part_sum = jnp.einsum(
            "hck,hkd->chd", weights, value_block, preferred_element_type=jnp.float32
        )
        return accum + part_sum.reshape(rows, local_heads * HEAD_SIZE)

    empty = jnp.zeros((rows, local_heads * HEAD_SIZE), jnp.float32)
    steps = total // block
    if steps == 1:
        return one_block(0, empty)
    return lax.fori_loop(0, steps, one_block, empty)


def finish(attended, gate, norm_gain):
    wide = attended.astype(jnp.float32)
    mean = jnp.mean(wide, axis=1, keepdims=True)
    var = jnp.mean((wide - mean) ** 2, axis=1, keepdims=True)
    normed = (wide - mean) * lax.rsqrt(var + 1e-05) * norm_gain[None, :]
    return (normed * gate.astype(jnp.float32)).astype(jnp.bfloat16)


def per_device(cands, kv_store, proj_weight, norm_gain, users, lengths):
    n_blk = lax.axis_size("blk")
    blk = lax.axis_index("blk")
    slot = lax.axis_index("store")
    person = lax.dynamic_index_in_dim(users, slot, 0, keepdims=False)
    count = lax.dynamic_index_in_dim(lengths, person, 0, keepdims=False)
    half = proj_weight.shape[2]
    local_heads = half // HEAD_SIZE

    n_users, n_pos = kv_store.shape[0], kv_store.shape[1]
    ordered = jnp.take(kv_store, users, axis=0).reshape(
        n_users, n_pos, 2, n_blk, local_heads, HEAD_SIZE
    )
    ordered = jnp.transpose(ordered, (3, 0, 2, 4, 1, 5)).reshape(
        n_blk * n_users, 2, local_heads, n_pos, HEAD_SIZE
    )
    mine = cands[0]
    rows = mine.shape[0]
    if n_blk == 2:
        swap = [(0, 1), (1, 0)]
        peer, ordered = lax.optimization_barrier((lax.ppermute(mine, "blk", swap), ordered))
    fetched = lax.all_to_all(
        ordered, ("blk", "store"), split_axis=0, concat_axis=3, tiled=True
    )
    keys = fetched[0, 0]
    values = fetched[0, 1]

    def project(feats):
        proj = jnp.einsum("cd,dkh->ckh", feats, proj_weight, preferred_element_type=jnp.float32).transpose(1, 0, 2)
        query = proj[0].astype(jnp.bfloat16).reshape(-1, local_heads, HEAD_SIZE)
        gate = jax.nn.silu(proj[1]).astype(jnp.bfloat16)
        return jnp.transpose(query, (1, 0, 2)), gate

    if n_blk == 2:
        query_own, gate_own = project(mine)
        query_peer, gate_peer = project(peer)
        sent = attend(query_peer, keys, values, count).astype(jnp.bfloat16)
        back = lax.ppermute(jnp.stack([sent, gate_peer]), "blk", swap)
        kept = attend(query_own, keys, values, count).astype(jnp.bfloat16)
        first = blk == 0
        attended = jnp.where(first, jnp.concatenate([kept, back[0]], axis=1),
                             jnp.concatenate([back[0], kept], axis=1))
        gate_full = jnp.where(first, jnp.concatenate([gate_own, back[1]], axis=1),
                              jnp.concatenate([back[1], gate_own], axis=1))
        return finish(attended, gate_full, norm_gain)[None]

    feats = lax.all_gather(mine, "blk", axis=0, tiled=True)
    query, gate = project(feats)
    attended = attend(query, keys, values, count).astype(jnp.bfloat16)
    both = jnp.stack([attended, gate]).reshape(2, n_blk, rows, half)
    own = lax.all_to_all(both, "blk", split_axis=1, concat_axis=3, tiled=True)
    own = own.reshape(2, rows, n_blk * half)
    return finish(own[0], own[1], norm_gain)[None]


def solution(mesh):
    in_specs = (
        P(("batch", "store"), "blk", None),
        P("batch", ("blk", "store"), None, None),
        P(None, None, "blk"),
        P(),
        P("batch"),
        P("batch"),
    )
    out_specs = P(("batch", "store"), "blk", None)
    return jax.shard_map(
        per_device, mesh=mesh, in_specs=in_specs, out_specs=out_specs, check_vma=False
    )
```

```python
import jax
import jax.numpy as jnp
from jax import lax
from jax.sharding import PartitionSpec as P
from jax.experimental import pallas as pl
from jax.experimental.pallas import tpu as pltpu

D = 1024
HEADS = 8
HEAD_SIZE = D // HEADS


def attend(qheads, keys, values, count):
    inverse = HEAD_SIZE ** (-0.5)
    local_heads, rows, _ = qheads.shape
    total = keys.shape[1]
    block = min(total, 512)
    scale_count = count.astype(jnp.float32)

    def one_block(index, accum):
        start = index * block
        key_block = lax.dynamic_slice_in_dim(keys, start, block, 1)
        value_block = lax.dynamic_slice_in_dim(values, start, block, 1)
        scores = (
            jnp.einsum("hcd,hkd->hck", qheads, key_block, preferred_element_type=jnp.float32)
            * inverse
        )
        live = (start + jnp.arange(block) < count).astype(jnp.float32)
        weights = (jax.nn.silu(scores) * live[None, None, :] / scale_count).astype(jnp.bfloat16)
        part_sum = jnp.einsum(
            "hck,hkd->chd", weights, value_block, preferred_element_type=jnp.float32
        )
        return accum + part_sum.reshape(rows, local_heads * HEAD_SIZE)

    empty = jnp.zeros((rows, local_heads * HEAD_SIZE), jnp.float32)
    steps = total // block
    if steps == 1:
        return one_block(0, empty)
    return lax.fori_loop(0, steps, one_block, empty)


def finish(attended, gate, norm_gain):
    wide = attended.astype(jnp.float32)
    mean = jnp.mean(wide, axis=1, keepdims=True)
    var = jnp.mean((wide - mean) ** 2, axis=1, keepdims=True)
    normed = (wide - mean) * lax.rsqrt(var + 1e-05) * norm_gain[None, :]
    return (normed * gate.astype(jnp.float32)).astype(jnp.bfloat16)


def take_users(kv_store, users):
    n_users = users.shape[0]

    def kernel(users_ref, kv_hbm, out_hbm, sems):
        copies = [
            pltpu.make_async_copy(kv_hbm.at[users_ref[s]], out_hbm.at[s], sems.at[s])
            for s in range(n_users)
        ]
        for copy in copies:
            copy.start()
        for copy in copies:
            copy.wait()

    return pl.pallas_call(
        kernel,
        out_shape=jax.ShapeDtypeStruct((n_users,) + kv_store.shape[1:], kv_store.dtype),
        grid_spec=pltpu.PrefetchScalarGridSpec(
            num_scalar_prefetch=1,
            grid=(1,),
            in_specs=[pl.BlockSpec(memory_space=pl.ANY)],
            out_specs=pl.BlockSpec(memory_space=pl.ANY),
            scratch_shapes=[pltpu.SemaphoreType.DMA((n_users,))],
        ),
    )(users, kv_store)


def per_device(cands, kv_store, proj_weight, norm_gain, users, lengths):
    n_blk = lax.axis_size("blk")
    blk = lax.axis_index("blk")
    slot = lax.axis_index("store")
    person = lax.dynamic_index_in_dim(users, slot, 0, keepdims=False)
    count = lax.dynamic_index_in_dim(lengths, person, 0, keepdims=False)
    half = proj_weight.shape[2]
    local_heads = half // HEAD_SIZE

    n_users, n_pos = kv_store.shape[0], kv_store.shape[1]
    ordered = take_users(kv_store, users).reshape(
        n_users, n_pos, 2, n_blk, local_heads, HEAD_SIZE
    )
    ordered = jnp.transpose(ordered, (3, 0, 2, 4, 1, 5)).reshape(
        n_blk * n_users, 2, local_heads, n_pos, HEAD_SIZE
    )
    mine = cands[0]
    rows = mine.shape[0]
    if n_blk == 2:
        swap = [(0, 1), (1, 0)]
        peer, ordered = lax.optimization_barrier((lax.ppermute(mine, "blk", swap), ordered))
    fetched = lax.all_to_all(
        ordered, ("blk", "store"), split_axis=0, concat_axis=3, tiled=True
    )
    keys = fetched[0, 0]
    values = fetched[0, 1]

    def project(feats):
        proj = jnp.einsum("cd,dkh->ckh", feats, proj_weight, preferred_element_type=jnp.float32).transpose(1, 0, 2)
        query = proj[0].astype(jnp.bfloat16).reshape(-1, local_heads, HEAD_SIZE)
        gate = jax.nn.silu(proj[1]).astype(jnp.bfloat16)
        return jnp.transpose(query, (1, 0, 2)), gate

    if n_blk == 2:
        query_own, gate_own = project(mine)
        query_peer, gate_peer = project(peer)
        sent = attend(query_peer, keys, values, count).astype(jnp.bfloat16)
        back = lax.ppermute(jnp.stack([sent, gate_peer]), "blk", swap)
        kept = attend(query_own, keys, values, count).astype(jnp.bfloat16)
        first = blk == 0
        attended = jnp.where(first, jnp.concatenate([kept, back[0]], axis=1),
                             jnp.concatenate([back[0], kept], axis=1))
        gate_full = jnp.where(first, jnp.concatenate([gate_own, back[1]], axis=1),
                              jnp.concatenate([back[1], gate_own], axis=1))
        return finish(attended, gate_full, norm_gain)[None]

    feats = lax.all_gather(mine, "blk", axis=0, tiled=True)
    query, gate = project(feats)
    attended = attend(query, keys, values, count).astype(jnp.bfloat16)
    both = jnp.stack([attended, gate]).reshape(2, n_blk, rows, half)
    own = lax.all_to_all(both, "blk", split_axis=1, concat_axis=3, tiled=True)
    own = own.reshape(2, rows, n_blk * half)
    return finish(own[0], own[1], norm_gain)[None]


def solution(mesh):
    in_specs = (
        P(("batch", "store"), "blk", None),
        P("batch", ("blk", "store"), None, None),
        P(None, None, "blk"),
        P(),
        P("batch"),
        P("batch"),
    )
    out_specs = P(("batch", "store"), "blk", None)
    return jax.shard_map(
        per_device, mesh=mesh, in_specs=in_specs, out_specs=out_specs, check_vma=False
    )
```

```python
import jax
import jax.numpy as jnp
from jax import lax
from jax.sharding import PartitionSpec as P

D = 1024
HEADS = 8
HEAD_SIZE = D // HEADS


def attend(qheads, keys, values, count):
    inverse = HEAD_SIZE ** (-0.5)
    local_heads, rows, _ = qheads.shape
    total = keys.shape[1]
    block = min(total, 512)
    scale_count = count.astype(jnp.float32)

    def one_block(index, accum):
        start = index * block
        key_block = lax.dynamic_slice_in_dim(keys, start, block, 1)
        value_block = lax.dynamic_slice_in_dim(values, start, block, 1)
        scores = (
            jnp.einsum("hcd,hkd->hck", qheads, key_block, preferred_element_type=jnp.float32)
            * inverse
        )
        live = (start + jnp.arange(block) < count).astype(jnp.float32)
        weights = (jax.nn.silu(scores) * live[None, None, :] / scale_count).astype(jnp.bfloat16)
        part_sum = jnp.einsum(
            "hck,hkd->chd", weights, value_block, preferred_element_type=jnp.float32
        )
        return accum + part_sum.reshape(rows, local_heads * HEAD_SIZE)

    empty = jnp.zeros((rows, local_heads * HEAD_SIZE), jnp.float32)
    steps = total // block
    if steps == 1:
        return one_block(0, empty)
    return lax.fori_loop(0, steps, one_block, empty)


def finish(attended, gate, norm_gain):
    wide = attended.astype(jnp.float32)
    mean = jnp.mean(wide, axis=1, keepdims=True)
    var = jnp.mean((wide - mean) ** 2, axis=1, keepdims=True)
    normed = (wide - mean) * lax.rsqrt(var + 1e-05) * norm_gain[None, :]
    return (normed * gate.astype(jnp.float32)).astype(jnp.bfloat16)


def per_device(cands, kv_store, proj_weight, norm_gain, users, lengths):
    n_blk = lax.axis_size("blk")
    blk = lax.axis_index("blk")
    slot = lax.axis_index("store")
    person = lax.dynamic_index_in_dim(users, slot, 0, keepdims=False)
    count = lax.dynamic_index_in_dim(lengths, person, 0, keepdims=False)
    half = proj_weight.shape[2]
    local_heads = half // HEAD_SIZE

    n_users, n_pos = kv_store.shape[0], kv_store.shape[1]
    ordered = jnp.take(kv_store, users, axis=0).reshape(
        n_users, n_pos, 2, n_blk, local_heads, HEAD_SIZE
    )
    ordered = jnp.transpose(ordered, (3, 0, 2, 4, 1, 5)).reshape(
        n_blk * n_users, 2, local_heads, n_pos, HEAD_SIZE
    )
    fetched = lax.all_to_all(
        ordered, ("blk", "store"), split_axis=0, concat_axis=3, tiled=True
    )
    keys = fetched[0, 0]
    values = fetched[0, 1]

    mine = cands[0]
    rows = mine.shape[0]

    def project(feats):
        proj = jnp.einsum("cd,dkh->kch", feats, proj_weight, preferred_element_type=jnp.float32)
        query = proj[0].astype(jnp.bfloat16).reshape(-1, local_heads, HEAD_SIZE)
        gate = jax.nn.silu(proj[1]).astype(jnp.bfloat16)
        return jnp.transpose(query, (1, 0, 2)), gate

    if n_blk == 2:
        swap = [(0, 1), (1, 0)]
        peer = lax.ppermute(mine, "blk", swap)
        query_own, gate_own = project(mine)
        query_peer, gate_peer = project(peer)
        gate_back = lax.ppermute(gate_peer, "blk", swap)
        sent = attend(query_peer, keys, values, count).astype(jnp.bfloat16)
        back = lax.ppermute(sent, "blk", swap)
        kept = attend(query_own, keys, values, count).astype(jnp.bfloat16)
        first = blk == 0
        attended = jnp.where(first, jnp.concatenate([kept, back], axis=1),
                             jnp.concatenate([back, kept], axis=1))
        gate_full = jnp.where(first, jnp.concatenate([gate_own, gate_back], axis=1),
                              jnp.concatenate([gate_back, gate_own], axis=1))
        return finish(attended, gate_full, norm_gain)[None]

    feats = lax.all_gather(mine, "blk", axis=0, tiled=True)
    query, gate = project(feats)
    attended = attend(query, keys, values, count).astype(jnp.bfloat16)
    both = jnp.stack([attended, gate]).reshape(2, n_blk, rows, half)
    own = lax.all_to_all(both, "blk", split_axis=1, concat_axis=3, tiled=True)
    own = own.reshape(2, rows, n_blk * half)
    return finish(own[0], own[1], norm_gain)[None]


def solution(mesh):
    in_specs = (
        P(("batch", "store"), "blk", None),
        P("batch", ("blk", "store"), None, None),
        P(None, None, "blk"),
        P(),
        P("batch"),
        P("batch"),
    )
    out_specs = P(("batch", "store"), "blk", None)
    return jax.shard_map(
        per_device, mesh=mesh, in_specs=in_specs, out_specs=out_specs, check_vma=False
    )
```

```python
import jax
import jax.numpy as jnp
from jax import lax
from jax.sharding import PartitionSpec as P

D = 1024
HEADS = 8
HEAD_SIZE = D // HEADS


def attend(qheads, keys, values, count):
    inverse = HEAD_SIZE ** (-0.5)
    local_heads, rows, _ = qheads.shape
    total = keys.shape[1]
    block = min(total, 512)
    scale_count = count.astype(jnp.float32)

    def one_block(index, accum):
        start = index * block
        key_block = lax.dynamic_slice_in_dim(keys, start, block, 1)
        value_block = lax.dynamic_slice_in_dim(values, start, block, 1)
        scores = (
            jnp.einsum("hcd,hkd->hck", qheads, key_block, preferred_element_type=jnp.float32)
            * inverse
        )
        live = (start + jnp.arange(block) < count).astype(jnp.float32)
        weights = (jax.nn.silu(scores) * live[None, None, :] / scale_count).astype(jnp.bfloat16)
        part_sum = jnp.einsum(
            "hck,hkd->chd", weights, value_block, preferred_element_type=jnp.float32
        )
        return accum + part_sum.reshape(rows, local_heads * HEAD_SIZE)

    empty = jnp.zeros((rows, local_heads * HEAD_SIZE), jnp.float32)
    steps = total // block
    if steps == 1:
        return one_block(0, empty)
    return lax.fori_loop(0, steps, one_block, empty)


def finish(attended, gate, norm_gain):
    wide = attended.astype(jnp.float32)
    mean = jnp.mean(wide, axis=1, keepdims=True)
    var = jnp.mean((wide - mean) ** 2, axis=1, keepdims=True)
    normed = (wide - mean) * lax.rsqrt(var + 1e-05) * norm_gain[None, :]
    return (normed * gate.astype(jnp.float32)).astype(jnp.bfloat16)


def per_device(cands, kv_store, proj_weight, norm_gain, users, lengths):
    n_blk = lax.axis_size("blk")
    blk = lax.axis_index("blk")
    slot = lax.axis_index("store")
    person = lax.dynamic_index_in_dim(users, slot, 0, keepdims=False)
    count = lax.dynamic_index_in_dim(lengths, person, 0, keepdims=False)
    half = proj_weight.shape[2]
    local_heads = half // HEAD_SIZE

    n_users, n_pos = kv_store.shape[0], kv_store.shape[1]
    count, kv_store = lax.optimization_barrier((count, kv_store))
    ordered = jnp.take(kv_store, users, axis=0).reshape(
        n_users, n_pos, 2, n_blk, local_heads, HEAD_SIZE
    )
    ordered = jnp.transpose(ordered, (3, 0, 2, 4, 1, 5)).reshape(
        n_blk * n_users, 2, local_heads, n_pos, HEAD_SIZE
    )
    fetched = lax.all_to_all(
        ordered, ("blk", "store"), split_axis=0, concat_axis=3, tiled=True
    )
    keys = fetched[0, 0]
    values = fetched[0, 1]

    mine = cands[0]
    rows = mine.shape[0]

    def project(feats):
        proj = jnp.einsum("cd,dkh->kch", feats, proj_weight, preferred_element_type=jnp.float32)
        query = proj[0].astype(jnp.bfloat16).reshape(-1, local_heads, HEAD_SIZE)
        gate = jax.nn.silu(proj[1]).astype(jnp.bfloat16)
        return jnp.transpose(query, (1, 0, 2)), gate

    if n_blk == 2:
        swap = [(0, 1), (1, 0)]
        peer = lax.ppermute(mine, "blk", swap)
        query_own, gate_own = project(mine)
        query_peer, gate_peer = project(peer)
        gate_back = lax.ppermute(gate_peer, "blk", swap)
        sent = attend(query_peer, keys, values, count).astype(jnp.bfloat16)
        back = lax.ppermute(sent, "blk", swap)
        kept = attend(query_own, keys, values, count).astype(jnp.bfloat16)
        first = blk == 0
        attended = jnp.where(first, jnp.concatenate([kept, back], axis=1),
                             jnp.concatenate([back, kept], axis=1))
        gate_full = jnp.where(first, jnp.concatenate([gate_own, gate_back], axis=1),
                              jnp.concatenate([gate_back, gate_own], axis=1))
        return finish(attended, gate_full, norm_gain)[None]

    feats = lax.all_gather(mine, "blk", axis=0, tiled=True)
    query, gate = project(feats)
    attended = attend(query, keys, values, count).astype(jnp.bfloat16)
    both = jnp.stack([attended, gate]).reshape(2, n_blk, rows, half)
    own = lax.all_to_all(both, "blk", split_axis=1, concat_axis=3, tiled=True)
    own = own.reshape(2, rows, n_blk * half)
    return finish(own[0], own[1], norm_gain)[None]


def solution(mesh):
    in_specs = (
        P(("batch", "store"), "blk", None),
        P("batch", ("blk", "store"), None, None),
        P(None, None, "blk"),
        P(),
        P("batch"),
        P("batch"),
    )
    out_specs = P(("batch", "store"), "blk", None)
    return jax.shard_map(
        per_device, mesh=mesh, in_specs=in_specs, out_specs=out_specs, check_vma=False
    )
```

```python
import jax
import jax.numpy as jnp
from jax import lax
from jax.sharding import PartitionSpec as P

D = 1024
HEADS = 8
HEAD_SIZE = D // HEADS


def attend(qheads, keys, values, count):
    inverse = HEAD_SIZE ** (-0.5)
    local_heads, rows, _ = qheads.shape
    total = keys.shape[1]
    block = min(total, 512)
    scale_count = count.astype(jnp.float32)

    def one_block(index, accum):
        start = index * block
        key_block = lax.dynamic_slice_in_dim(keys, start, block, 1)
        value_block = lax.dynamic_slice_in_dim(values, start, block, 1)
        scores = (
            jnp.einsum("hcd,hkd->hck", qheads, key_block, preferred_element_type=jnp.float32)
            * inverse
        )
        live = (start + jnp.arange(block) < count).astype(jnp.float32)
        weights = (jax.nn.silu(scores) * live[None, None, :] / scale_count).astype(jnp.bfloat16)
        part_sum = jnp.einsum(
            "hck,hkd->chd", weights, value_block, preferred_element_type=jnp.float32
        )
        return accum + part_sum.reshape(rows, local_heads * HEAD_SIZE)

    empty = jnp.zeros((rows, local_heads * HEAD_SIZE), jnp.float32)
    steps = total // block
    if steps == 1:
        return one_block(0, empty)
    return lax.fori_loop(0, steps, one_block, empty)


def finish(attended, gate, norm_gain):
    wide = attended.astype(jnp.float32)
    mean = jnp.mean(wide, axis=1, keepdims=True)
    var = jnp.mean((wide - mean) ** 2, axis=1, keepdims=True)
    normed = (wide - mean) * lax.rsqrt(var + 1e-05) * norm_gain[None, :]
    return (normed * gate.astype(jnp.float32)).astype(jnp.bfloat16)


def per_device(cands, kv_store, proj_weight, norm_gain, users, lengths):
    n_blk = lax.axis_size("blk")
    blk = lax.axis_index("blk")
    slot = lax.axis_index("store")
    person = lax.dynamic_index_in_dim(users, slot, 0, keepdims=False)
    count = lax.dynamic_index_in_dim(lengths, person, 0, keepdims=False)
    half = proj_weight.shape[2]
    local_heads = half // HEAD_SIZE

    n_users, n_pos = kv_store.shape[0], kv_store.shape[1]
    ordered = jnp.take(kv_store, users, axis=0).reshape(
        n_users, n_pos, 2, n_blk, local_heads, HEAD_SIZE
    )
    ordered = jnp.transpose(ordered, (3, 0, 2, 4, 1, 5)).reshape(
        n_blk * n_users, 2, local_heads, n_pos, HEAD_SIZE
    )
    fetched = lax.all_to_all(
        ordered, ("blk", "store"), split_axis=0, concat_axis=3, tiled=True
    )
    keys = fetched[0, 0]
    values = fetched[0, 1]

    mine = cands[0]
    rows = mine.shape[0]

    def project(feats):
        proj = jnp.dot(
            feats, proj_weight.reshape(proj_weight.shape[0], 2 * half),
            preferred_element_type=jnp.float32,
        ).reshape(feats.shape[0], 2, half)
        proj = jnp.transpose(proj, (1, 0, 2))
        query = proj[0].astype(jnp.bfloat16).reshape(-1, local_heads, HEAD_SIZE)
        gate = jax.nn.silu(proj[1]).astype(jnp.bfloat16)
        return jnp.transpose(query, (1, 0, 2)), gate

    if n_blk == 2:
        swap = [(0, 1), (1, 0)]
        peer = lax.ppermute(mine, "blk", swap)
        query_own, gate_own = project(mine)
        query_peer, gate_peer = project(peer)
        gate_back = lax.ppermute(gate_peer, "blk", swap)
        sent = attend(query_peer, keys, values, count).astype(jnp.bfloat16)
        back = lax.ppermute(sent, "blk", swap)
        kept = attend(query_own, keys, values, count).astype(jnp.bfloat16)
        first = blk == 0
        attended = jnp.where(first, jnp.concatenate([kept, back], axis=1),
                             jnp.concatenate([back, kept], axis=1))
        gate_full = jnp.where(first, jnp.concatenate([gate_own, gate_back], axis=1),
                              jnp.concatenate([gate_back, gate_own], axis=1))
        return finish(attended, gate_full, norm_gain)[None]

    feats = lax.all_gather(mine, "blk", axis=0, tiled=True)
    query, gate = project(feats)
    attended = attend(query, keys, values, count).astype(jnp.bfloat16)
    both = jnp.stack([attended, gate]).reshape(2, n_blk, rows, half)
    own = lax.all_to_all(both, "blk", split_axis=1, concat_axis=3, tiled=True)
    own = own.reshape(2, rows, n_blk * half)
    return finish(own[0], own[1], norm_gain)[None]


def solution(mesh):
    in_specs = (
        P(("batch", "store"), "blk", None),
        P("batch", ("blk", "store"), None, None),
        P(None, None, "blk"),
        P(),
        P("batch"),
        P("batch"),
    )
    out_specs = P(("batch", "store"), "blk", None)
    return jax.shard_map(
        per_device, mesh=mesh, in_specs=in_specs, out_specs=out_specs, check_vma=False
    )
```

```python
import jax
import jax.numpy as jnp
from jax import lax
from jax.sharding import PartitionSpec as P

D = 1024
HEADS = 8
HEAD_SIZE = D // HEADS


def attend(qheads, keys, values, count):
    inverse = HEAD_SIZE ** (-0.5)
    local_heads, rows, _ = qheads.shape
    total = keys.shape[1]
    block = min(total, 512)
    scale_count = count.astype(jnp.float32)

    def one_block(index, accum):
        start = index * block
        key_block = lax.dynamic_slice_in_dim(keys, start, block, 1)
        value_block = lax.dynamic_slice_in_dim(values, start, block, 1)
        scores = (
            jnp.einsum("hcd,hkd->hck", qheads, key_block, preferred_element_type=jnp.float32)
            * inverse
        )
        live = (start + jnp.arange(block) < count).astype(jnp.float32)
        weights = (jax.nn.silu(scores) * live[None, None, :] / scale_count).astype(jnp.bfloat16)
        part_sum = jnp.einsum(
            "hck,hkd->chd", weights, value_block, preferred_element_type=jnp.float32
        )
        return accum + part_sum.reshape(rows, local_heads * HEAD_SIZE)

    empty = jnp.zeros((rows, local_heads * HEAD_SIZE), jnp.float32)
    steps = total // block
    if steps == 1:
        return one_block(0, empty)
    return lax.fori_loop(0, steps, one_block, empty)


def finish(attended, gate, norm_gain):
    wide = attended.astype(jnp.float32)
    mean = jnp.mean(wide, axis=1, keepdims=True)
    var = jnp.mean((wide - mean) ** 2, axis=1, keepdims=True)
    normed = (wide - mean) * lax.rsqrt(var + 1e-05) * norm_gain[None, :]
    return (normed * gate.astype(jnp.float32)).astype(jnp.bfloat16)


def per_device(cands, kv_store, proj_weight, norm_gain, users, lengths):
    n_blk = lax.axis_size("blk")
    blk = lax.axis_index("blk")
    slot = lax.axis_index("store")
    person = lax.dynamic_index_in_dim(users, slot, 0, keepdims=False)
    count = lax.dynamic_index_in_dim(lengths, person, 0, keepdims=False)
    half = proj_weight.shape[2]
    local_heads = half // HEAD_SIZE

    n_users, n_pos = kv_store.shape[0], kv_store.shape[1]
    ordered = jnp.take(kv_store, users, axis=0).reshape(
        n_users, n_pos, 2, n_blk, local_heads, HEAD_SIZE
    )
    ordered = jnp.transpose(ordered, (3, 0, 2, 4, 1, 5)).reshape(
        n_blk * n_users, 2, local_heads, n_pos, HEAD_SIZE
    )
    fetched = lax.all_to_all(
        ordered, ("blk", "store"), split_axis=0, concat_axis=3, tiled=True
    )
    keys = fetched[0, 0]
    values = fetched[0, 1]

    mine = cands[0]
    rows = mine.shape[0]

    def project(feats):
        query = jnp.dot(feats, proj_weight[:, 0, :], preferred_element_type=jnp.float32)
        query = query.astype(jnp.bfloat16).reshape(-1, local_heads, HEAD_SIZE)
        gate = jnp.dot(feats, proj_weight[:, 1, :], preferred_element_type=jnp.float32)
        gate = jax.nn.silu(gate).astype(jnp.bfloat16)
        return jnp.transpose(query, (1, 0, 2)), gate

    if n_blk == 2:
        swap = [(0, 1), (1, 0)]
        peer = lax.ppermute(mine, "blk", swap)
        query_own, gate_own = project(mine)
        query_peer, gate_peer = project(peer)
        gate_back = lax.ppermute(gate_peer, "blk", swap)
        sent = attend(query_peer, keys, values, count).astype(jnp.bfloat16)
        back = lax.ppermute(sent, "blk", swap)
        kept = attend(query_own, keys, values, count).astype(jnp.bfloat16)
        first = blk == 0
        attended = jnp.where(first, jnp.concatenate([kept, back], axis=1),
                             jnp.concatenate([back, kept], axis=1))
        gate_full = jnp.where(first, jnp.concatenate([gate_own, gate_back], axis=1),
                              jnp.concatenate([gate_back, gate_own], axis=1))
        return finish(attended, gate_full, norm_gain)[None]

    feats = lax.all_gather(mine, "blk", axis=0, tiled=True)
    query, gate = project(feats)
    attended = attend(query, keys, values, count).astype(jnp.bfloat16)
    both = jnp.stack([attended, gate]).reshape(2, n_blk, rows, half)
    own = lax.all_to_all(both, "blk", split_axis=1, concat_axis=3, tiled=True)
    own = own.reshape(2, rows, n_blk * half)
    return finish(own[0], own[1], norm_gain)[None]


def solution(mesh):
    in_specs = (
        P(("batch", "store"), "blk", None),
        P("batch", ("blk", "store"), None, None),
        P(None, None, "blk"),
        P(),
        P("batch"),
        P("batch"),
    )
    out_specs = P(("batch", "store"), "blk", None)
    return jax.shard_map(
        per_device, mesh=mesh, in_specs=in_specs, out_specs=out_specs, check_vma=False
    )
```

```python
import jax
import jax.numpy as jnp
from jax import lax
from jax.sharding import PartitionSpec as P

D = 1024
HEADS = 8
HEAD_SIZE = D // HEADS


def attend(qheads, keys, values, count):
    inverse = HEAD_SIZE ** (-0.5)
    local_heads, rows, _ = qheads.shape
    total = keys.shape[1]
    block = min(total, 512)
    scale_count = count.astype(jnp.float32)

    def one_block(index, accum):
        start = index * block
        key_block = lax.dynamic_slice_in_dim(keys, start, block, 1)
        value_block = lax.dynamic_slice_in_dim(values, start, block, 1)
        scores = (
            jnp.einsum("hcd,hkd->hck", qheads, key_block, preferred_element_type=jnp.float32)
            * inverse
        )
        live = (start + jnp.arange(block) < count).astype(jnp.float32)
        weights = (jax.nn.silu(scores) * live[None, None, :] / scale_count).astype(jnp.bfloat16)
        part_sum = jnp.einsum(
            "hck,hkd->chd", weights, value_block, preferred_element_type=jnp.float32
        )
        return accum + part_sum.reshape(rows, local_heads * HEAD_SIZE)

    empty = jnp.zeros((rows, local_heads * HEAD_SIZE), jnp.float32)
    steps = total // block
    if steps == 1:
        return one_block(0, empty)
    return lax.fori_loop(0, steps, one_block, empty)


def finish(attended, gate, norm_gain):
    wide = attended.astype(jnp.float32)
    mean = jnp.mean(wide, axis=1, keepdims=True)
    var = jnp.mean((wide - mean) ** 2, axis=1, keepdims=True)
    normed = (wide - mean) * lax.rsqrt(var + 1e-05) * norm_gain[None, :]
    return (normed * gate.astype(jnp.float32)).astype(jnp.bfloat16)


def per_device(cands, kv_store, proj_weight, norm_gain, users, lengths):
    n_blk = lax.axis_size("blk")
    blk = lax.axis_index("blk")
    slot = lax.axis_index("store")
    person = lax.dynamic_index_in_dim(users, slot, 0, keepdims=False)
    count = lax.dynamic_index_in_dim(lengths, person, 0, keepdims=False)
    half = proj_weight.shape[2]
    local_heads = half // HEAD_SIZE

    n_users, n_pos = kv_store.shape[0], kv_store.shape[1]
    chosen = jnp.concatenate(
        [lax.dynamic_index_in_dim(kv_store, users[s], 0) for s in range(users.shape[0])]
    )
    ordered = chosen.reshape(
        n_users, n_pos, 2, n_blk, local_heads, HEAD_SIZE
    )
    ordered = jnp.transpose(ordered, (3, 0, 2, 4, 1, 5)).reshape(
        n_blk * n_users, 2, local_heads, n_pos, HEAD_SIZE
    )
    fetched = lax.all_to_all(
        ordered, ("blk", "store"), split_axis=0, concat_axis=3, tiled=True
    )
    keys = fetched[0, 0]
    values = fetched[0, 1]

    mine = cands[0]
    rows = mine.shape[0]

    def project(feats):
        proj = jnp.einsum("cd,dkh->kch", feats, proj_weight, preferred_element_type=jnp.float32)
        query = proj[0].astype(jnp.bfloat16).reshape(-1, local_heads, HEAD_SIZE)
        gate = jax.nn.silu(proj[1]).astype(jnp.bfloat16)
        return jnp.transpose(query, (1, 0, 2)), gate

    if n_blk == 2:
        swap = [(0, 1), (1, 0)]
        peer = lax.ppermute(mine, "blk", swap)
        query_own, gate_own = project(mine)
        query_peer, gate_peer = project(peer)
        gate_back = lax.ppermute(gate_peer, "blk", swap)
        sent = attend(query_peer, keys, values, count).astype(jnp.bfloat16)
        back = lax.ppermute(sent, "blk", swap)
        kept = attend(query_own, keys, values, count).astype(jnp.bfloat16)
        first = blk == 0
        attended = jnp.where(first, jnp.concatenate([kept, back], axis=1),
                             jnp.concatenate([back, kept], axis=1))
        gate_full = jnp.where(first, jnp.concatenate([gate_own, gate_back], axis=1),
                              jnp.concatenate([gate_back, gate_own], axis=1))
        return finish(attended, gate_full, norm_gain)[None]

    feats = lax.all_gather(mine, "blk", axis=0, tiled=True)
    query, gate = project(feats)
    attended = attend(query, keys, values, count).astype(jnp.bfloat16)
    both = jnp.stack([attended, gate]).reshape(2, n_blk, rows, half)
    own = lax.all_to_all(both, "blk", split_axis=1, concat_axis=3, tiled=True)
    own = own.reshape(2, rows, n_blk * half)
    return finish(own[0], own[1], norm_gain)[None]


def solution(mesh):
    in_specs = (
        P(("batch", "store"), "blk", None),
        P("batch", ("blk", "store"), None, None),
        P(None, None, "blk"),
        P(),
        P("batch"),
        P("batch"),
    )
    out_specs = P(("batch", "store"), "blk", None)
    return jax.shard_map(
        per_device, mesh=mesh, in_specs=in_specs, out_specs=out_specs, check_vma=False
    )
```

```python
import jax
import jax.numpy as jnp
from jax import lax
from jax.sharding import PartitionSpec as P

D = 1024
HEADS = 8
HEAD_SIZE = D // HEADS


def attend(qheads, keys, values, count):
    inverse = HEAD_SIZE ** (-0.5)
    local_heads, rows, _ = qheads.shape
    total = keys.shape[1]
    block = min(total, 512)
    scale_count = count.astype(jnp.float32)

    def one_block(index, accum):
        start = index * block
        key_block = lax.dynamic_slice_in_dim(keys, start, block, 1)
        value_block = lax.dynamic_slice_in_dim(values, start, block, 1)
        scores = (
            jnp.einsum("hcd,hkd->hck", qheads, key_block, preferred_element_type=jnp.float32)
            * inverse
        )
        live = (start + jnp.arange(block) < count).astype(jnp.float32)
        weights = (jax.nn.silu(scores) * live[None, None, :] / scale_count).astype(jnp.bfloat16)
        part_sum = jnp.einsum(
            "hck,hkd->chd", weights, value_block, preferred_element_type=jnp.float32
        )
        return accum + part_sum.reshape(rows, local_heads * HEAD_SIZE)

    empty = jnp.zeros((rows, local_heads * HEAD_SIZE), jnp.float32)
    steps = total // block
    if steps == 1:
        return one_block(0, empty)
    return lax.fori_loop(0, steps, one_block, empty)


def finish(attended, gate, norm_gain):
    wide = attended.astype(jnp.float32)
    mean = jnp.mean(wide, axis=1, keepdims=True)
    var = jnp.mean((wide - mean) ** 2, axis=1, keepdims=True)
    normed = (wide - mean) * lax.rsqrt(var + 1e-05) * norm_gain[None, :]
    return (normed * gate.astype(jnp.float32)).astype(jnp.bfloat16)


def per_device(cands, kv_store, proj_weight, norm_gain, users, lengths):
    n_blk = lax.axis_size("blk")
    blk = lax.axis_index("blk")
    slot = lax.axis_index("store")
    person = lax.dynamic_index_in_dim(users, slot, 0, keepdims=False)
    count = lax.dynamic_index_in_dim(lengths, person, 0, keepdims=False)
    half = proj_weight.shape[2]
    local_heads = half // HEAD_SIZE

    n_users, n_pos = kv_store.shape[0], kv_store.shape[1]
    ordered = jnp.take(kv_store, users, axis=0).reshape(
        n_users, n_pos, 2, n_blk, local_heads, HEAD_SIZE
    )
    ordered = jnp.transpose(ordered, (3, 0, 2, 4, 1, 5)).reshape(
        n_blk * n_users, 2, local_heads, n_pos, HEAD_SIZE
    )
    fetched = lax.all_to_all(
        ordered, ("blk", "store"), split_axis=0, concat_axis=3, tiled=True
    )
    keys = fetched[0, 0]
    values = fetched[0, 1]

    mine = cands[0]
    rows = mine.shape[0]

    def project(feats):
        proj = jnp.einsum("cd,dkh->kch", feats, proj_weight, preferred_element_type=jnp.float32)
        query = proj[0].astype(jnp.bfloat16).reshape(-1, local_heads, HEAD_SIZE)
        return jnp.transpose(query, (1, 0, 2)), proj[1]

    if n_blk == 2:
        swap = [(0, 1), (1, 0)]
        peer = lax.ppermute(mine, "blk", swap)
        query_own, gate_own = project(mine)
        query_peer, gate_peer = project(peer)
        gate_back = lax.ppermute(jax.nn.silu(gate_peer).astype(jnp.bfloat16), "blk", swap)
        sent = attend(query_peer, keys, values, count).astype(jnp.bfloat16)
        back = lax.ppermute(sent, "blk", swap)
        query_own, gate_own, _ = lax.optimization_barrier((query_own, gate_own, sent))
        gate_own = jax.nn.silu(gate_own).astype(jnp.bfloat16)
        kept = attend(query_own, keys, values, count).astype(jnp.bfloat16)
        first = blk == 0
        attended = jnp.where(first, jnp.concatenate([kept, back], axis=1),
                             jnp.concatenate([back, kept], axis=1))
        gate_full = jnp.where(first, jnp.concatenate([gate_own, gate_back], axis=1),
                              jnp.concatenate([gate_back, gate_own], axis=1))
        return finish(attended, gate_full, norm_gain)[None]

    feats = lax.all_gather(mine, "blk", axis=0, tiled=True)
    query, gate = project(feats)
    gate = jax.nn.silu(gate).astype(jnp.bfloat16)
    attended = attend(query, keys, values, count).astype(jnp.bfloat16)
    both = jnp.stack([attended, gate]).reshape(2, n_blk, rows, half)
    own = lax.all_to_all(both, "blk", split_axis=1, concat_axis=3, tiled=True)
    own = own.reshape(2, rows, n_blk * half)
    return finish(own[0], own[1], norm_gain)[None]


def solution(mesh):
    in_specs = (
        P(("batch", "store"), "blk", None),
        P("batch", ("blk", "store"), None, None),
        P(None, None, "blk"),
        P(),
        P("batch"),
        P("batch"),
    )
    out_specs = P(("batch", "store"), "blk", None)
    return jax.shard_map(
        per_device, mesh=mesh, in_specs=in_specs, out_specs=out_specs, check_vma=False
    )
```

```python
import jax
import jax.numpy as jnp
from jax import lax
from jax.sharding import PartitionSpec as P

D = 1024
HEADS = 8
HEAD_SIZE = D // HEADS


def attend(qheads, keys, values, count):
    inverse = HEAD_SIZE ** (-0.5)
    local_heads, rows, _ = qheads.shape
    total = keys.shape[1]
    block = min(total, 512)
    scale_count = count.astype(jnp.float32)

    def one_block(index, accum):
        start = index * block
        key_block = lax.dynamic_slice_in_dim(keys, start, block, 1)
        value_block = lax.dynamic_slice_in_dim(values, start, block, 1)
        scores = (
            jnp.einsum("hcd,hkd->hck", qheads, key_block, preferred_element_type=jnp.float32)
            * inverse
        )
        live = (start + jnp.arange(block) < count).astype(jnp.float32)
        weights = (jax.nn.silu(scores) * live[None, None, :] / scale_count).astype(jnp.bfloat16)
        part_sum = jnp.einsum(
            "hck,hkd->chd", weights, value_block, preferred_element_type=jnp.float32
        )
        return accum + part_sum.reshape(rows, local_heads * HEAD_SIZE)

    empty = jnp.zeros((rows, local_heads * HEAD_SIZE), jnp.float32)
    steps = total // block
    if steps == 1:
        return one_block(0, empty)
    return lax.fori_loop(0, steps, one_block, empty)


def finish(attended, gate, norm_gain):
    wide = attended.astype(jnp.float32)
    mean = jnp.mean(wide, axis=1, keepdims=True)
    var = jnp.mean((wide - mean) ** 2, axis=1, keepdims=True)
    normed = (wide - mean) * lax.rsqrt(var + 1e-05) * norm_gain[None, :]
    return (normed * gate.astype(jnp.float32)).astype(jnp.bfloat16)


def per_device(cands, kv_store, proj_weight, norm_gain, users, lengths):
    n_blk = lax.axis_size("blk")
    blk = lax.axis_index("blk")
    slot = lax.axis_index("store")
    person = lax.dynamic_index_in_dim(users, slot, 0, keepdims=False)
    count = lax.dynamic_index_in_dim(lengths, person, 0, keepdims=False)
    half = proj_weight.shape[2]
    local_heads = half // HEAD_SIZE

    n_users, n_pos = kv_store.shape[0], kv_store.shape[1]
    ordered = kv_store.at[users].get(mode="promise_in_bounds", unique_indices=True).reshape(
        n_users, n_pos, 2, n_blk, local_heads, HEAD_SIZE
    )
    ordered = jnp.transpose(ordered, (3, 0, 2, 4, 1, 5)).reshape(
        n_blk * n_users, 2, local_heads, n_pos, HEAD_SIZE
    )
    fetched = lax.all_to_all(
        ordered, ("blk", "store"), split_axis=0, concat_axis=3, tiled=True
    )
    keys = fetched[0, 0]
    values = fetched[0, 1]

    mine = cands[0]
    rows = mine.shape[0]

    def project(feats):
        proj = jnp.einsum("cd,dkh->kch", feats, proj_weight, preferred_element_type=jnp.float32)
        query = proj[0].astype(jnp.bfloat16).reshape(-1, local_heads, HEAD_SIZE)
        gate = jax.nn.silu(proj[1]).astype(jnp.bfloat16)
        return jnp.transpose(query, (1, 0, 2)), gate

    if n_blk == 2:
        swap = [(0, 1), (1, 0)]
        peer = lax.ppermute(mine, "blk", swap)
        query_own, gate_own = project(mine)
        query_peer, gate_peer = project(peer)
        gate_back = lax.ppermute(gate_peer, "blk", swap)
        sent = attend(query_peer, keys, values, count).astype(jnp.bfloat16)
        back = lax.ppermute(sent, "blk", swap)
        kept = attend(query_own, keys, values, count).astype(jnp.bfloat16)
        first = blk == 0
        attended = jnp.where(first, jnp.concatenate([kept, back], axis=1),
                             jnp.concatenate([back, kept], axis=1))
        gate_full = jnp.where(first, jnp.concatenate([gate_own, gate_back], axis=1),
                              jnp.concatenate([gate_back, gate_own], axis=1))
        return finish(attended, gate_full, norm_gain)[None]

    feats = lax.all_gather(mine, "blk", axis=0, tiled=True)
    query, gate = project(feats)
    attended = attend(query, keys, values, count).astype(jnp.bfloat16)
    both = jnp.stack([attended, gate]).reshape(2, n_blk, rows, half)
    own = lax.all_to_all(both, "blk", split_axis=1, concat_axis=3, tiled=True)
    own = own.reshape(2, rows, n_blk * half)
    return finish(own[0], own[1], norm_gain)[None]


def solution(mesh):
    in_specs = (
        P(("batch", "store"), "blk", None),
        P("batch", ("blk", "store"), None, None),
        P(None, None, "blk"),
        P(),
        P("batch"),
        P("batch"),
    )
    out_specs = P(("batch", "store"), "blk", None)
    return jax.shard_map(
        per_device, mesh=mesh, in_specs=in_specs, out_specs=out_specs, check_vma=False
    )
```

```python
import jax
import jax.numpy as jnp
from jax import lax
from jax.sharding import PartitionSpec as P

D = 1024
HEADS = 8
HEAD_SIZE = D // HEADS


def attend(qheads, keys, values, count):
    inverse = HEAD_SIZE ** (-0.5)
    local_heads, rows, _ = qheads.shape
    total = keys.shape[1]
    block = min(total, 512)
    scale_count = count.astype(jnp.float32)

    def one_block(index, accum):
        start = index * block
        key_block = lax.dynamic_slice_in_dim(keys, start, block, 1)
        value_block = lax.dynamic_slice_in_dim(values, start, block, 1)
        scores = (
            jnp.einsum("hcd,hkd->hck", qheads, key_block, preferred_element_type=jnp.float32)
            * inverse
        )
        live = (start + jnp.arange(block) < count).astype(jnp.float32)
        weights = (jax.nn.silu(scores) * live[None, None, :] / scale_count).astype(jnp.bfloat16)
        part_sum = jnp.einsum(
            "hck,hkd->chd", weights, value_block, preferred_element_type=jnp.float32
        )
        return accum + part_sum.reshape(rows, local_heads * HEAD_SIZE)

    empty = jnp.zeros((rows, local_heads * HEAD_SIZE), jnp.float32)
    steps = total // block
    if steps == 1:
        return one_block(0, empty)
    return lax.fori_loop(0, steps, one_block, empty)


def finish(attended, gate, norm_gain):
    wide = attended.astype(jnp.float32)
    mean = jnp.mean(wide, axis=1, keepdims=True)
    var = jnp.mean((wide - mean) ** 2, axis=1, keepdims=True)
    normed = (wide - mean) * lax.rsqrt(var + 1e-05) * norm_gain[None, :]
    return (normed * gate.astype(jnp.float32)).astype(jnp.bfloat16)


def per_device(cands, kv_store, proj_weight, norm_gain, users, lengths):
    n_blk = lax.axis_size("blk")
    blk = lax.axis_index("blk")
    slot = lax.axis_index("store")
    ids = jnp.arange(users.shape[0], dtype=jnp.int32)
    chosen = (ids[:, None] == slot) & (users[:, None] == ids[None, :])
    count = jnp.sum(jnp.where(chosen, lengths[None, :], 0))
    half = proj_weight.shape[2]
    local_heads = half // HEAD_SIZE

    n_users, n_pos = kv_store.shape[0], kv_store.shape[1]
    ordered = kv_store.at[users].get(mode="promise_in_bounds", unique_indices=True).reshape(
        n_users, n_pos, 2, n_blk, local_heads, HEAD_SIZE
    )
    ordered = jnp.transpose(ordered, (3, 0, 2, 4, 1, 5)).reshape(
        n_blk * n_users, 2, local_heads, n_pos, HEAD_SIZE
    )
    fetched = lax.all_to_all(
        ordered, ("blk", "store"), split_axis=0, concat_axis=3, tiled=True
    )
    keys = fetched[0, 0]
    values = fetched[0, 1]

    mine = cands[0]
    rows = mine.shape[0]

    def project(feats):
        proj = jnp.einsum("cd,dkh->kch", feats, proj_weight, preferred_element_type=jnp.float32)
        query = proj[0].astype(jnp.bfloat16).reshape(-1, local_heads, HEAD_SIZE)
        gate = jax.nn.silu(proj[1]).astype(jnp.bfloat16)
        return jnp.transpose(query, (1, 0, 2)), gate

    if n_blk == 2:
        swap = [(0, 1), (1, 0)]
        peer = lax.ppermute(mine, "blk", swap)
        query_own, gate_own = project(mine)
        query_peer, gate_peer = project(peer)
        gate_back = lax.ppermute(gate_peer, "blk", swap)
        sent = attend(query_peer, keys, values, count).astype(jnp.bfloat16)
        back = lax.ppermute(sent, "blk", swap)
        kept = attend(query_own, keys, values, count).astype(jnp.bfloat16)
        first = blk == 0
        attended = jnp.where(first, jnp.concatenate([kept, back], axis=1),
                             jnp.concatenate([back, kept], axis=1))
        gate_full = jnp.where(first, jnp.concatenate([gate_own, gate_back], axis=1),
                              jnp.concatenate([gate_back, gate_own], axis=1))
        return finish(attended, gate_full, norm_gain)[None]

    feats = lax.all_gather(mine, "blk", axis=0, tiled=True)
    query, gate = project(feats)
    attended = attend(query, keys, values, count).astype(jnp.bfloat16)
    both = jnp.stack([attended, gate]).reshape(2, n_blk, rows, half)
    own = lax.all_to_all(both, "blk", split_axis=1, concat_axis=3, tiled=True)
    own = own.reshape(2, rows, n_blk * half)
    return finish(own[0], own[1], norm_gain)[None]


def solution(mesh):
    in_specs = (
        P(("batch", "store"), "blk", None),
        P("batch", ("blk", "store"), None, None),
        P(None, None, "blk"),
        P(),
        P("batch"),
        P("batch"),
    )
    out_specs = P(("batch", "store"), "blk", None)
    return jax.shard_map(
        per_device, mesh=mesh, in_specs=in_specs, out_specs=out_specs, check_vma=False
    )
```

```python
import jax
import jax.numpy as jnp
from jax import lax
from jax.sharding import PartitionSpec as P

D = 1024
HEADS = 8
HEAD_SIZE = D // HEADS


def attend(qheads, keys, values, count):
    inverse = HEAD_SIZE ** (-0.5)
    local_heads, rows, _ = qheads.shape
    total = keys.shape[1]
    block = min(total, 512)
    scale_count = count.astype(jnp.float32)

    def one_block(index, accum):
        start = index * block
        key_block = lax.dynamic_slice_in_dim(keys, start, block, 1)
        value_block = lax.dynamic_slice_in_dim(values, start, block, 1)
        scores = (
            jnp.einsum("hcd,hkd->hck", qheads, key_block, preferred_element_type=jnp.float32)
            * inverse
        )
        live = (start + jnp.arange(block) < count).astype(jnp.float32)
        weights = (jax.nn.silu(scores) * live[None, None, :] / scale_count).astype(jnp.bfloat16)
        part_sum = jnp.einsum(
            "hck,hkd->chd", weights, value_block, preferred_element_type=jnp.float32
        )
        return accum + part_sum.reshape(rows, local_heads * HEAD_SIZE)

    empty = jnp.zeros((rows, local_heads * HEAD_SIZE), jnp.float32)
    steps = total // block
    if steps == 1:
        return one_block(0, empty)
    return lax.fori_loop(0, steps, one_block, empty)


def finish(attended, gate, norm_gain):
    wide = attended.astype(jnp.float32)
    mean = jnp.mean(wide, axis=1, keepdims=True)
    var = jnp.mean((wide - mean) ** 2, axis=1, keepdims=True)
    normed = (wide - mean) * lax.rsqrt(var + 1e-05) * norm_gain[None, :]
    return (normed * gate.astype(jnp.float32)).astype(jnp.bfloat16)


def per_device(cands, kv_store, proj_weight, norm_gain, users, lengths):
    n_blk = lax.axis_size("blk")
    blk = lax.axis_index("blk")
    slot = lax.axis_index("store")
    ids = jnp.arange(users.shape[0], dtype=jnp.int32)
    chosen = (ids[:, None] == slot) & (users[:, None] == ids[None, :])
    count = jnp.sum(jnp.where(chosen, lengths[None, :], 0))
    half = proj_weight.shape[2]
    local_heads = half // HEAD_SIZE

    n_users, n_pos = kv_store.shape[0], kv_store.shape[1]
    ordered = kv_store.at[users].get(mode="promise_in_bounds", unique_indices=True).reshape(
        n_users, n_pos, 2, n_blk, local_heads, HEAD_SIZE
    )
    ordered = jnp.transpose(ordered, (3, 0, 2, 4, 1, 5)).reshape(
        n_blk * n_users, 2, local_heads, n_pos, HEAD_SIZE
    )
    fetched = lax.all_to_all(
        ordered, ("blk", "store"), split_axis=0, concat_axis=3, tiled=True
    )
    keys = fetched[0, 0]
    values = fetched[0, 1]

    mine = cands[0]
    rows = mine.shape[0]

    def project(feats):
        proj = jnp.einsum("cd,dkh->kch", feats, proj_weight, preferred_element_type=jnp.float32)
        query = proj[0].astype(jnp.bfloat16).reshape(-1, local_heads, HEAD_SIZE)
        gate = jax.nn.silu(proj[1]).astype(jnp.bfloat16)
        return jnp.transpose(query, (1, 0, 2)), gate

    if n_blk == 2:
        swap = [(0, 1), (1, 0)]
        peer = lax.ppermute(mine, "blk", swap)
        query_peer, gate_peer = project(peer)
        gate_back = lax.ppermute(gate_peer, "blk", swap)
        sent = attend(query_peer, keys, values, count).astype(jnp.bfloat16)
        back = lax.ppermute(sent, "blk", swap)
        late, _ = lax.optimization_barrier((mine, sent))
        query_own, gate_own = project(late)
        kept = attend(query_own, keys, values, count).astype(jnp.bfloat16)
        first = blk == 0
        attended = jnp.where(first, jnp.concatenate([kept, back], axis=1),
                             jnp.concatenate([back, kept], axis=1))
        gate_full = jnp.where(first, jnp.concatenate([gate_own, gate_back], axis=1),
                              jnp.concatenate([gate_back, gate_own], axis=1))
        return finish(attended, gate_full, norm_gain)[None]

    feats = lax.all_gather(mine, "blk", axis=0, tiled=True)
    query, gate = project(feats)
    attended = attend(query, keys, values, count).astype(jnp.bfloat16)
    both = jnp.stack([attended, gate]).reshape(2, n_blk, rows, half)
    own = lax.all_to_all(both, "blk", split_axis=1, concat_axis=3, tiled=True)
    own = own.reshape(2, rows, n_blk * half)
    return finish(own[0], own[1], norm_gain)[None]


def solution(mesh):
    in_specs = (
        P(("batch", "store"), "blk", None),
        P("batch", ("blk", "store"), None, None),
        P(None, None, "blk"),
        P(),
        P("batch"),
        P("batch"),
    )
    out_specs = P(("batch", "store"), "blk", None)
    return jax.shard_map(
        per_device, mesh=mesh, in_specs=in_specs, out_specs=out_specs, check_vma=False
    )
```

```python
import jax
import jax.numpy as jnp
from jax import lax
from jax.sharding import PartitionSpec as P
from jax.experimental.layout import Layout, with_layout_constraint

D = 1024
HEADS = 8
HEAD_SIZE = D // HEADS


def attend(qheads, keys, values, count):
    inverse = HEAD_SIZE ** (-0.5)
    local_heads, rows, _ = qheads.shape
    total = keys.shape[1]
    block = min(total, 512)
    scale_count = count.astype(jnp.float32)

    def one_block(index, accum):
        start = index * block
        key_block = lax.dynamic_slice_in_dim(keys, start, block, 1)
        value_block = lax.dynamic_slice_in_dim(values, start, block, 1)
        scores = (
            jnp.einsum("hcd,hkd->hck", qheads, key_block, preferred_element_type=jnp.float32)
            * inverse
        )
        live = (start + jnp.arange(block) < count).astype(jnp.float32)
        weights = (jax.nn.silu(scores) * live[None, None, :] / scale_count).astype(jnp.bfloat16)
        part_sum = jnp.einsum(
            "hck,hkd->chd", weights, value_block, preferred_element_type=jnp.float32
        )
        return accum + part_sum.reshape(rows, local_heads * HEAD_SIZE)

    empty = jnp.zeros((rows, local_heads * HEAD_SIZE), jnp.float32)
    steps = total // block
    if steps == 1:
        return one_block(0, empty)
    return lax.fori_loop(0, steps, one_block, empty)


def finish(attended, gate, norm_gain):
    wide = attended.astype(jnp.float32)
    mean = jnp.mean(wide, axis=1, keepdims=True)
    var = jnp.mean((wide - mean) ** 2, axis=1, keepdims=True)
    normed = (wide - mean) * lax.rsqrt(var + 1e-05) * norm_gain[None, :]
    return (normed * gate.astype(jnp.float32)).astype(jnp.bfloat16)


def per_device(cands, kv_store, proj_weight, norm_gain, users, lengths):
    n_blk = lax.axis_size("blk")
    blk = lax.axis_index("blk")
    slot = lax.axis_index("store")
    ids = jnp.arange(users.shape[0], dtype=jnp.int32)
    chosen = (ids[:, None] == slot) & (users[:, None] == ids[None, :])
    count = jnp.sum(jnp.where(chosen, lengths[None, :], 0))
    half = proj_weight.shape[2]
    local_heads = half // HEAD_SIZE

    n_users, n_pos = kv_store.shape[0], kv_store.shape[1]
    ordered = kv_store.at[users].get(mode="promise_in_bounds", unique_indices=True).reshape(
        n_users, n_pos, 2, n_blk, local_heads, HEAD_SIZE
    )
    ordered = jnp.transpose(ordered, (3, 0, 2, 4, 1, 5)).reshape(
        n_blk * n_users, 2, local_heads, n_pos, HEAD_SIZE
    )
    fetched = lax.all_to_all(
        ordered, ("blk", "store"), split_axis=0, concat_axis=3, tiled=True
    )
    keys = fetched[0, 0]
    values = fetched[0, 1]

    mine = cands[0]
    rows = mine.shape[0]

    def project(feats):
        proj = jnp.einsum("cd,dkh->kch", feats, proj_weight, preferred_element_type=jnp.float32)
        query = proj[0].astype(jnp.bfloat16).reshape(-1, local_heads, HEAD_SIZE)
        gate = jax.nn.silu(proj[1]).astype(jnp.bfloat16)
        return jnp.transpose(query, (1, 0, 2)), gate

    if n_blk == 2:
        swap = [(0, 1), (1, 0)]
        peer = lax.ppermute(mine, "blk", swap)
        query_own, gate_own = project(mine)
        query_peer, gate_peer = project(peer)
        gate_back = lax.ppermute(gate_peer, "blk", swap)
        row_major = Layout(major_to_minor=(0, 1))
        sent = attend(query_peer, keys, values, count).astype(jnp.bfloat16)
        sent = with_layout_constraint(sent, row_major)
        back = lax.ppermute(sent, "blk", swap)
        query_own, gate_own, _ = lax.optimization_barrier((query_own, gate_own, sent))
        kept = attend(query_own, keys, values, count).astype(jnp.bfloat16)
        kept = with_layout_constraint(kept, row_major)
        first = blk == 0
        attended = jnp.where(first, jnp.concatenate([kept, back], axis=1),
                             jnp.concatenate([back, kept], axis=1))
        gate_full = jnp.where(first, jnp.concatenate([gate_own, gate_back], axis=1),
                              jnp.concatenate([gate_back, gate_own], axis=1))
        return finish(attended, gate_full, norm_gain)[None]

    feats = lax.all_gather(mine, "blk", axis=0, tiled=True)
    query, gate = project(feats)
    attended = attend(query, keys, values, count).astype(jnp.bfloat16)
    both = jnp.stack([attended, gate]).reshape(2, n_blk, rows, half)
    own = lax.all_to_all(both, "blk", split_axis=1, concat_axis=3, tiled=True)
    own = own.reshape(2, rows, n_blk * half)
    return finish(own[0], own[1], norm_gain)[None]


def solution(mesh):
    in_specs = (
        P(("batch", "store"), "blk", None),
        P("batch", ("blk", "store"), None, None),
        P(None, None, "blk"),
        P(),
        P("batch"),
        P("batch"),
    )
    out_specs = P(("batch", "store"), "blk", None)
    return jax.shard_map(
        per_device, mesh=mesh, in_specs=in_specs, out_specs=out_specs, check_vma=False
    )
```

```python
import jax
import jax.numpy as jnp
from jax import lax
from jax.sharding import PartitionSpec as P

D = 1024
HEADS = 8
HEAD_SIZE = D // HEADS


def attend(qheads, keys, values, positions, count):
    inverse = HEAD_SIZE ** (-0.5)
    local_heads, rows, _ = qheads.shape
    total = keys.shape[1]
    block = min(total, 512)
    scale_count = count.astype(jnp.float32)

    def one_block(index, accum):
        start = index * block
        key_block = lax.dynamic_slice_in_dim(keys, start, block, 1)
        value_block = lax.dynamic_slice_in_dim(values, start, block, 1)
        scores = (
            jnp.einsum("hcd,hkd->hck", qheads, key_block, preferred_element_type=jnp.float32)
            * inverse
        )
        live = (lax.dynamic_slice_in_dim(positions, start, block) < count).astype(jnp.float32)
        weights = (jax.nn.silu(scores) * live[None, None, :] / scale_count).astype(jnp.bfloat16)
        part_sum = jnp.einsum(
            "hck,hkd->chd", weights, value_block, preferred_element_type=jnp.float32
        )
        return accum + part_sum.reshape(rows, local_heads * HEAD_SIZE)

    empty = jnp.zeros((rows, local_heads * HEAD_SIZE), jnp.float32)
    steps = total // block
    if steps == 1:
        return one_block(0, empty)
    return lax.fori_loop(0, steps, one_block, empty)


def finish(attended, gate, norm_gain):
    wide = attended.astype(jnp.float32)
    mean = jnp.mean(wide, axis=1, keepdims=True)
    var = jnp.mean((wide - mean) ** 2, axis=1, keepdims=True)
    normed = (wide - mean) * lax.rsqrt(var + 1e-05) * norm_gain[None, :]
    return (normed * gate.astype(jnp.float32)).astype(jnp.bfloat16)


def per_device(cands, kv_store, proj_weight, norm_gain, users, lengths):
    n_blk = lax.axis_size("blk")
    blk = lax.axis_index("blk")
    slot = lax.axis_index("store")
    ids = jnp.arange(users.shape[0], dtype=jnp.int32)
    chosen = (ids[:, None] == slot) & (users[:, None] == ids[None, :])
    count = jnp.sum(jnp.where(chosen, lengths[None, :], 0))
    half = proj_weight.shape[2]
    local_heads = half // HEAD_SIZE

    n_users, n_pos = kv_store.shape[0], kv_store.shape[1]
    ordered = kv_store.at[users].get(mode="promise_in_bounds", unique_indices=True).reshape(
        n_users, n_pos, 2, n_blk, local_heads, HEAD_SIZE
    )
    group = n_blk * n_users
    if group <= 8:
        ordered = jnp.transpose(ordered, (0, 3, 2, 4, 1, 5)).reshape(
            group, 2, local_heads, n_pos, HEAD_SIZE
        )
        me = slot * n_blk + blk
        rotated = jnp.roll(ordered, -me, axis=0)
        pieces = [rotated[0]]
        for k in range(1, group):
            shift = [(i, (i + k) % group) for i in range(group)]
            pieces.append(lax.ppermute(rotated[k], ("store", "blk"), shift))
        fetched = jnp.stack(pieces, axis=2).reshape(2, local_heads, group * n_pos, HEAD_SIZE)
        sender = (me - jnp.arange(group, dtype=jnp.int32)) % group
        source = (sender % n_blk) * n_users + sender // n_blk
    else:
        ordered = jnp.transpose(ordered, (3, 0, 2, 4, 1, 5)).reshape(
            group, 2, local_heads, n_pos, HEAD_SIZE
        )
        fetched = lax.all_to_all(
            ordered, ("blk", "store"), split_axis=0, concat_axis=3, tiled=True
        )[0]
        source = jnp.arange(group, dtype=jnp.int32)
    positions = (source[:, None] * n_pos + jnp.arange(n_pos, dtype=jnp.int32)[None, :]).reshape(-1)
    keys = fetched[0]
    values = fetched[1]

    mine = cands[0]
    rows = mine.shape[0]

    def project(feats):
        proj = jnp.einsum("cd,dkh->kch", feats, proj_weight, preferred_element_type=jnp.float32)
        query = proj[0].astype(jnp.bfloat16).reshape(-1, local_heads, HEAD_SIZE)
        gate = jax.nn.silu(proj[1]).astype(jnp.bfloat16)
        return jnp.transpose(query, (1, 0, 2)), gate

    if n_blk == 2:
        swap = [(0, 1), (1, 0)]
        peer = lax.ppermute(mine, "blk", swap)
        query_own, gate_own = project(mine)
        query_peer, gate_peer = project(peer)
        gate_back = lax.ppermute(gate_peer, "blk", swap)
        sent = attend(query_peer, keys, values, positions, count).astype(jnp.bfloat16)
        back = lax.ppermute(sent, "blk", swap)
        kept = attend(query_own, keys, values, positions, count).astype(jnp.bfloat16)
        first = blk == 0
        attended = jnp.where(first, jnp.concatenate([kept, back], axis=1),
                             jnp.concatenate([back, kept], axis=1))
        gate_full = jnp.where(first, jnp.concatenate([gate_own, gate_back], axis=1),
                              jnp.concatenate([gate_back, gate_own], axis=1))
        return finish(attended, gate_full, norm_gain)[None]

    feats = lax.all_gather(mine, "blk", axis=0, tiled=True)
    query, gate = project(feats)
    attended = attend(query, keys, values, positions, count).astype(jnp.bfloat16)
    both = jnp.stack([attended, gate]).reshape(2, n_blk, rows, half)
    own = lax.all_to_all(both, "blk", split_axis=1, concat_axis=3, tiled=True)
    own = own.reshape(2, rows, n_blk * half)
    return finish(own[0], own[1], norm_gain)[None]


def solution(mesh):
    in_specs = (
        P(("batch", "store"), "blk", None),
        P("batch", ("blk", "store"), None, None),
        P(None, None, "blk"),
        P(),
        P("batch"),
        P("batch"),
    )
    out_specs = P(("batch", "store"), "blk", None)
    return jax.shard_map(
        per_device, mesh=mesh, in_specs=in_specs, out_specs=out_specs, check_vma=False
    )
```

```python
import jax
import jax.numpy as jnp
from jax import lax
from jax.sharding import PartitionSpec as P

D = 1024
HEADS = 8
HEAD_SIZE = D // HEADS


def attend(qheads, keys, values, count):
    inverse = HEAD_SIZE ** (-0.5)
    local_heads, rows, _ = qheads.shape
    total = keys.shape[1]
    block = min(total, 512)
    scale_count = count.astype(jnp.float32)

    def one_block(index, accum):
        start = index * block
        key_block = lax.dynamic_slice_in_dim(keys, start, block, 1)
        value_block = lax.dynamic_slice_in_dim(values, start, block, 1)
        scores = (
            jnp.einsum("hcd,hkd->hck", qheads, key_block, preferred_element_type=jnp.float32)
            * inverse
        )
        live = (start + jnp.arange(block) < count).astype(jnp.float32)
        weights = (jax.nn.silu(scores) * live[None, None, :] / scale_count).astype(jnp.bfloat16)
        part_sum = jnp.einsum(
            "hck,hkd->chd", weights, value_block, preferred_element_type=jnp.float32
        )
        return accum + part_sum.reshape(rows, local_heads * HEAD_SIZE)

    empty = jnp.zeros((rows, local_heads * HEAD_SIZE), jnp.float32)
    steps = total // block
    if steps == 1:
        return one_block(0, empty)
    return lax.fori_loop(0, steps, one_block, empty)


def finish(attended, gate, norm_gain):
    wide = attended.astype(jnp.float32)
    mean = jnp.mean(wide, axis=1, keepdims=True)
    var = jnp.mean((wide - mean) ** 2, axis=1, keepdims=True)
    normed = (wide - mean) * lax.rsqrt(var + 1e-05) * norm_gain[None, :]
    return (normed * gate.astype(jnp.float32)).astype(jnp.bfloat16)


def per_device(cands, kv_store, proj_weight, norm_gain, users, lengths):
    n_blk = lax.axis_size("blk")
    blk = lax.axis_index("blk")
    slot = lax.axis_index("store")
    ids = jnp.arange(users.shape[0], dtype=jnp.int32)
    chosen = (ids[:, None] == slot) & (users[:, None] == ids[None, :])
    count = jnp.sum(jnp.where(chosen, lengths[None, :], 0))
    half = proj_weight.shape[2]
    local_heads = half // HEAD_SIZE

    n_users, n_pos = kv_store.shape[0], kv_store.shape[1]
    ordered = lax.gather(
        kv_store, users[:, None],
        lax.GatherDimensionNumbers(
            offset_dims=(1, 2, 3), collapsed_slice_dims=(0,), start_index_map=(0,)
        ),
        (1,) + kv_store.shape[1:],
        unique_indices=True,
        mode=lax.GatherScatterMode.PROMISE_IN_BOUNDS,
    ).reshape(
        n_users, n_pos, 2, n_blk, local_heads, HEAD_SIZE
    )
    ordered = jnp.transpose(ordered, (3, 0, 2, 4, 1, 5)).reshape(
        n_blk * n_users, 2, local_heads, n_pos, HEAD_SIZE
    )
    fetched = lax.all_to_all(
        ordered, ("blk", "store"), split_axis=0, concat_axis=3, tiled=True
    )
    keys = fetched[0, 0]
    values = fetched[0, 1]

    mine = cands[0]
    rows = mine.shape[0]

    def project(feats):
        proj = jnp.einsum("cd,dkh->kch", feats, proj_weight, preferred_element_type=jnp.float32)
        query = proj[0].astype(jnp.bfloat16).reshape(-1, local_heads, HEAD_SIZE)
        gate = jax.nn.silu(proj[1]).astype(jnp.bfloat16)
        return jnp.transpose(query, (1, 0, 2)), gate

    if n_blk == 2:
        swap = [(0, 1), (1, 0)]
        peer = lax.ppermute(mine, "blk", swap)
        query_own, gate_own = project(mine)
        query_peer, gate_peer = project(peer)
        gate_back = lax.ppermute(gate_peer, "blk", swap)
        sent = attend(query_peer, keys, values, count).astype(jnp.bfloat16)
        back = lax.ppermute(sent, "blk", swap)
        kept = attend(query_own, keys, values, count).astype(jnp.bfloat16)
        first = blk == 0
        attended = jnp.where(first, jnp.concatenate([kept, back], axis=1),
                             jnp.concatenate([back, kept], axis=1))
        gate_full = jnp.where(first, jnp.concatenate([gate_own, gate_back], axis=1),
                              jnp.concatenate([gate_back, gate_own], axis=1))
        return finish(attended, gate_full, norm_gain)[None]

    feats = lax.all_gather(mine, "blk", axis=0, tiled=True)
    query, gate = project(feats)
    attended = attend(query, keys, values, count).astype(jnp.bfloat16)
    both = jnp.stack([attended, gate]).reshape(2, n_blk, rows, half)
    own = lax.all_to_all(both, "blk", split_axis=1, concat_axis=3, tiled=True)
    own = own.reshape(2, rows, n_blk * half)
    return finish(own[0], own[1], norm_gain)[None]


def solution(mesh):
    in_specs = (
        P(("batch", "store"), "blk", None),
        P("batch", ("blk", "store"), None, None),
        P(None, None, "blk"),
        P(),
        P("batch"),
        P("batch"),
    )
    out_specs = P(("batch", "store"), "blk", None)
    return jax.shard_map(
        per_device, mesh=mesh, in_specs=in_specs, out_specs=out_specs, check_vma=False
    )
```
